128 devices in a mesh: redist: 32 (over x, y, core), rep: 4 (over z).
Axes of the slice: x: 4, y: 4, z: 4, core: 2. Of those that a mesh axis runs over, the one named last changes fastest.
Arguments:
- amplitudes: bfloat16 [4, 128, 1024, 1024], P(None, ('redist', 'rep')), may hold values from -6 to 6
- integrals: bfloat16 [128, 1024, 2, 1024], P(None, 'redist'), may hold values from -0.046875 to 0.046875
- occ_irrep: int32 [128], replicated, may hold values from 0 to 7, as said below
- virt_irrep: int32 [1024], replicated, may hold values from 0 to 7, as said below
Outputs:
- cycle_term: float32 [4, 1024, 2, 1024], P(None, None, None, 'redist')
The draws below stay inside these ranges and needn't reach their ends.
Inputs may be any that keep to these rules, and one draw needn't show every extreme that they name: `occ_irrep`: labels never fall along the orbitals; each of the 8 irreps holds one contiguous range of between n // 16 and 3 * n // 16 orbitals, n being 128 or 1024. `virt_irrep`: labels never fall along the orbitals; each of the 8 irreps holds one contiguous range of between n // 16 and 3 * n // 16 orbitals, n being 128 or 1024.
All inputs are finite; a program needn't handle non-finite values.
Results may differ from the reference program's by a relative error of at most 0.0003.
Values may be sent and summed in bfloat16 or wider, within the bound.
No kernel may reach another device: no remote copies, remote signals or barrier semaphores. Data moves between devices by JAX's collectives and lax.ppermute only.
A program may use at most 192 MiB of HBM per device.

```python
import jax
import jax.numpy as jnp
from jax import lax

O = 128
V = 1024
ISLAB = 4
JSLAB = 2


def contiguous_labels(key, count):
    base = jnp.arange(1, 8, dtype=jnp.int32) * count // 8
    jitter = jax.random.randint(key, (7,), -(count // 32), count // 32 + 1, dtype=jnp.int32)
    cuts = base + jitter
    places = jnp.arange(count, dtype=jnp.int32)
    return jnp.sum((places[:, None] >= cuts[None, :]).astype(jnp.int32), axis=1).astype(jnp.int32)


def draw_occ_irrep(key, part):
    return contiguous_labels(jax.random.fold_in(key, 11), O)


def draw_virt_irrep(key, part):
    return contiguous_labels(jax.random.fold_in(key, 23), V)


def level_of(rng, dims, shards, smallest, top_value):
    def one(dim, shards_of):
        steps = jax.random.uniform(jax.random.fold_in(jax.random.fold_in(rng, 6), dim), (shards_of,), jnp.float32, smallest / len(shards), top_value / len(shards))
        return jnp.repeat(jnp.exp(steps), dims[dim] // shards_of).reshape((-1,) + (1,) * (len(dims) - dim - 1))

    gain = one(*shards[0])
    for cut in shards[1:]:
        gain = gain * one(*cut)
    return gain


def noise(own_key, dims, spread, bound, cuts=(), kind=jnp.bfloat16):
    array = spread * jax.random.normal(own_key, dims, jnp.float32)
    if cuts:
        array = array * level_of(own_key, dims, cuts, -0.22, 0.18)
    return jnp.clip(array, -bound, bound).astype(kind)


def setup_inputs(seed: int = 0) -> dict:
    arg_keys = jax.random.split(jax.random.key(seed), 5)
    amplitudes = noise(arg_keys[0], (ISLAB, O, V, V), 1.0, 6.0, ((1, 128),))
    integrals = noise(arg_keys[1], (O, V, JSLAB, V), (O * V // 8) ** -0.5, 0.046875, ((1, 32),))
    occ_irrep = draw_occ_irrep(jax.random.fold_in(arg_keys[4], 71), 0)
    virt_irrep = draw_virt_irrep(jax.random.fold_in(arg_keys[4], 71), 0)
    return dict(amplitudes=amplitudes, integrals=integrals, occ_irrep=occ_irrep, virt_irrep=virt_irrep)


def reference(amplitudes, integrals, occ_irrep, virt_irrep):
    occ_rows = occ_irrep[:ISLAB]
    occ_js = occ_irrep[:JSLAB]
    pair_ac = jnp.bitwise_xor(virt_irrep[:, None], virt_irrep[None, :])
    pair_jb = jnp.bitwise_xor(occ_js[:, None], virt_irrep[None, :])

    def advance(total, k_index):
        amp_slice = lax.dynamic_index_in_dim(amplitudes, k_index, 1, keepdims=False)
        k_label = lax.dynamic_index_in_dim(occ_irrep, k_index, 0, keepdims=False)
        pair_ik = jnp.bitwise_xor(occ_rows, k_label)
        allowed = pair_ik[:, None, None] == pair_ac[None, :, :]
        amp_slice = jnp.where(allowed, amp_slice, jnp.zeros((), amp_slice.dtype))
        int_slice = lax.dynamic_index_in_dim(integrals, k_index, 0, keepdims=False)
        pair_kc = jnp.bitwise_xor(k_label, virt_irrep)
        sym_ok = pair_kc[:, None, None] == pair_jb[None, :, :]
        int_slice = jnp.where(sym_ok, int_slice, jnp.zeros((), int_slice.dtype))
        total = total + jnp.dot(amp_slice.reshape(ISLAB * V, V), int_slice.reshape(V, JSLAB * V), preferred_element_type=jnp.float32)
        return total, None

    total, _ = lax.scan(advance, jnp.zeros((ISLAB * V, JSLAB * V), jnp.float32), jnp.arange(O, dtype=jnp.int32))
    return total.reshape(ISLAB, V, JSLAB, V)
```

```python
import jax
import jax.numpy as jnp
from jax import lax
from jax.sharding import PartitionSpec as P

N_IRREPS = 8


def irrep_windows(virt_irrep, width):
    count = virt_irrep.shape[0]
    starts = jnp.sum(
        (virt_irrep[None, :] < jnp.arange(N_IRREPS, dtype=virt_irrep.dtype)[:, None]).astype(jnp.int32),
        axis=1,
    )
    return jnp.minimum(starts, count - width)


def parts_in(span, count):
    return min(N_IRREPS, -(-span // (count // 16)) + 1)


def body(amplitudes, integrals, occ_irrep, virt_irrep):
    n_redist = lax.axis_size("redist")
    n_rep = lax.axis_size("rep")
    dev_index = lax.axis_index("redist")
    rep_index = lax.axis_index("rep")
    i_slab, k_block, v_width, _ = amplitudes.shape
    c_block = integrals.shape[1]
    j_slab = integrals.shape[2]
    width = 3 * v_width // 16
    wins = irrep_windows(virt_irrep, width)
    occ_rows = occ_irrep[:i_slab]
    occ_js = occ_irrep[:j_slab]

    grouped = integrals.reshape(n_redist, n_rep, k_block, c_block, j_slab, v_width)
    mine = lax.dynamic_index_in_dim(grouped, rep_index, 1, keepdims=False)
    mine = mine.reshape(n_redist * k_block, c_block, j_slab, v_width)
    dest_k = (
        (jnp.arange(n_redist, dtype=jnp.int32)[:, None] * n_rep + rep_index) * k_block
        + jnp.arange(k_block, dtype=jnp.int32)[None, :]
    ).reshape(-1)
    dest_lab = occ_irrep[dest_k]
    c_lab = lax.dynamic_slice_in_dim(virt_irrep, dev_index * c_block, c_block)
    n_cparts = parts_in(c_block, v_width)
    pieces = []
    for d in range(n_redist * k_block):
        row = mine[d]
        piece = jnp.zeros((c_block, j_slab, width), integrals.dtype)
        for p in range(n_cparts):
            lab = jnp.minimum(c_lab[0] + p, N_IRREPS - 1)
            start = wins[jnp.bitwise_xor(lab, dest_lab[d])]
            cut = lax.dynamic_slice_in_dim(row, start, width, axis=2)
            piece = jnp.where((c_lab == c_lab[0] + p)[:, None, None], cut, piece)
        pieces.append(piece)
    packed = jnp.stack(pieces)
    moved = lax.all_to_all(packed, "redist", split_axis=0, concat_axis=1, tiled=True)
    moved = moved.reshape(k_block, n_redist * c_block, j_slab, width)

    my_k0 = (dev_index * n_rep + rep_index) * k_block
    blocks = []
    for kk in range(k_block):
        k_lab = occ_irrep[my_k0 + kk]
        amp = amplitudes[:, kk]
        ints = moved[kk]
        pair_ik = jnp.bitwise_xor(occ_rows, k_lab)
        per_g = []
        for g in range(N_IRREPS):
            c_irrep = jnp.bitwise_xor(g, k_lab)
            wa = wins[g]
            wc = wins[c_irrep]
            a_lab = lax.dynamic_slice_in_dim(virt_irrep, wa, width)
            cw_lab = lax.dynamic_slice_in_dim(virt_irrep, wc, width)
            a_blk = lax.dynamic_slice(amp, (0, wa, wc), (i_slab, width, width))
            allowed = pair_ik[:, None, None] == jnp.bitwise_xor(a_lab[:, None], cw_lab[None, :])[None]
            a_blk = jnp.where(allowed, a_blk, jnp.zeros((), a_blk.dtype))
            i_blk = lax.dynamic_slice_in_dim(ints, wc, width, axis=0)
            sym = (cw_lab == c_irrep)[:, None, None] & (
                jnp.bitwise_xor(cw_lab, k_lab)[:, None, None]
                == jnp.bitwise_xor(occ_js[:, None], a_lab[None, :])[None]
            )
            i_blk = jnp.where(sym, i_blk, jnp.zeros((), i_blk.dtype))
            blk = lax.dot_general(
                i_blk, a_blk, (((0,), (2,)), ((), ())), preferred_element_type=jnp.float32
            )
            per_g.append(jnp.transpose(blk, (1, 0, 2, 3)).reshape(width, -1))
        blocks.append(jnp.concatenate(per_g, axis=0))
    every = blocks[0]
    for more in blocks[1:]:
        every = every + more
    b_pos = jnp.arange(v_width, dtype=jnp.int32)
    pick = virt_irrep * width + (b_pos - wins[virt_irrep])
    compact = jnp.take(every, pick, axis=0)

    shares = lax.psum_scatter(compact, ("redist", "rep"), scatter_dimension=0, tiled=True)
    mine_b = lax.all_gather(shares, "rep", axis=0, tiled=True)

    nb = mine_b.shape[0]
    b_lab = lax.dynamic_slice_in_dim(virt_irrep, dev_index * nb, nb)
    vals = mine_b.reshape(nb, j_slab, i_slab, width).transpose(2, 3, 1, 0)
    out = jnp.zeros((i_slab, v_width, j_slab, nb), jnp.float32)
    for p in range(parts_in(nb, v_width)):
        lab = b_lab[0] + p
        part = jnp.where((b_lab == lab)[None, None, None, :], vals, 0.0)
        start = wins[jnp.minimum(lab, N_IRREPS - 1)]
        placed = lax.dynamic_update_slice(
            jnp.zeros((i_slab, v_width, j_slab, nb), jnp.float32), part, (0, start, 0, 0)
        )
        out = out + placed
    return out


def solution(mesh):
    placed = (P(None, ("redist", "rep"), None, None), P(None, "redist", None, None), P(), P())
    return jax.shard_map(
        body, mesh=mesh, in_specs=placed, out_specs=P(None, None, None, "redist"), check_vma=False
    )
```

```python
import jax
import jax.numpy as jnp
from jax import lax
from jax.sharding import PartitionSpec as P

N_IRREPS = 8


def irrep_windows(virt_irrep, width):
    count = virt_irrep.shape[0]
    starts = jnp.sum(
        (virt_irrep[None, :] < jnp.arange(N_IRREPS, dtype=virt_irrep.dtype)[:, None]).astype(jnp.int32),
        axis=1,
    )
    return jnp.minimum(starts, count - width)


def parts_in(span, count):
    return min(N_IRREPS, -(-span // (count // 16)) + 1)


def shifted_pick(array, axis, width, wins, choice):
    out = None
    for g in range(N_IRREPS):
        cut = lax.dynamic_slice_in_dim(array, wins[g], width, axis=axis)
        out = cut if out is None else jnp.where(choice == g, cut, out)
    return out


def body(amplitudes, integrals, occ_irrep, virt_irrep):
    n_redist = lax.axis_size("redist")
    n_rep = lax.axis_size("rep")
    dev_index = lax.axis_index("redist")
    rep_index = lax.axis_index("rep")
    i_slab, k_block, v_width, _ = amplitudes.shape
    c_block = integrals.shape[1]
    j_slab = integrals.shape[2]
    if k_block != 1 or i_slab % n_rep:
        raise ValueError("unsupported split")
    i_per = i_slab // n_rep
    width = 3 * v_width // 16
    wins = irrep_windows(virt_irrep, width)
    occ_rows = occ_irrep[:i_slab]
    occ_js = occ_irrep[:j_slab]
    zero_bf = jnp.zeros((), amplitudes.dtype)

    my_k = dev_index * n_rep + rep_index
    my_lab = occ_irrep[my_k]
    a_win = jnp.bitwise_xor(virt_irrep, my_lab)
    amp = amplitudes[:, 0]
    amp_c = shifted_pick(amp, 2, width, wins, a_win[None, :, None])
    c_lab = shifted_pick(
        jnp.broadcast_to(virt_irrep[None, :], (v_width, v_width)), 1, width, wins, a_win[:, None]
    )
    allowed = jnp.bitwise_xor(occ_rows, my_lab)[:, None, None] == jnp.bitwise_xor(
        virt_irrep[:, None], c_lab
    )[None]
    amp_c = jnp.where(allowed, amp_c, zero_bf)
    amp_c = amp_c.reshape(n_rep, i_per, 1, v_width, width)
    amp_g = lax.all_to_all(amp_c, "rep", split_axis=0, concat_axis=2, tiled=True)[0]

    all_k_lab = occ_irrep[: integrals.shape[0]]
    my_c_lab = lax.dynamic_slice_in_dim(virt_irrep, dev_index * c_block, c_block)
    b_win = jnp.bitwise_xor(all_k_lab[:, None], my_c_lab[None, :])
    ints_c = shifted_pick(integrals, 3, width, wins, b_win[:, :, None, None])
    b_lab = shifted_pick(
        jnp.broadcast_to(virt_irrep, b_win.shape + (v_width,)), 2, width, wins, b_win[:, :, None]
    )
    sym = jnp.bitwise_xor(all_k_lab[:, None], my_c_lab[None, :])[:, :, None, None] == jnp.bitwise_xor(
        occ_js[None, None, :, None], b_lab[:, :, None, :]
    )
    ints_c = jnp.where(sym, ints_c, zero_bf)
    ints_c = ints_c.reshape(n_redist, n_rep, c_block, j_slab, width)
    ints_g = lax.all_to_all(ints_c, "redist", split_axis=0, concat_axis=2, tiled=True)[0]

    group_lab = occ_irrep[dev_index * n_rep + jnp.arange(n_rep, dtype=jnp.int32)]
    per_g = []
    for g in range(N_IRREPS):
        wa = wins[g]
        row_lab = lax.dynamic_slice_in_dim(virt_irrep, wa, width)
        a_parts = []
        i_parts = []
        for kk in range(n_rep):
            c_irrep = jnp.bitwise_xor(g, group_lab[kk])
            wc = wins[c_irrep]
            a_blk = lax.dynamic_slice_in_dim(amp_g[:, kk], wa, width, axis=1)
            a_parts.append(jnp.where((row_lab == g)[None, :, None], a_blk, zero_bf))
            cw_lab = lax.dynamic_slice_in_dim(virt_irrep, wc, width)
            i_blk = lax.dynamic_slice_in_dim(ints_g[kk], wc, width, axis=0)
            i_parts.append(jnp.where((cw_lab == c_irrep)[:, None, None], i_blk, zero_bf))
        a_cat = jnp.concatenate(a_parts, axis=2)
        i_cat = jnp.concatenate(i_parts, axis=0)
        blk = lax.dot_general(
            i_cat, a_cat, (((0,), (2,)), ((), ())), preferred_element_type=jnp.float32
        )
        per_g.append(jnp.transpose(blk, (1, 0, 2, 3)).reshape(width, -1))
    every = jnp.concatenate(per_g, axis=0)
    b_pos = jnp.arange(v_width, dtype=jnp.int32)
    pick = virt_irrep * width + (b_pos - wins[virt_irrep])
    compact = jnp.take(every, pick, axis=0)

    nb = v_width // n_redist
    pieces = lax.all_to_all(compact.reshape(n_redist, nb, -1), "redist", 0, 0, tiled=True)
    summed = jnp.sum(pieces, axis=0)
    mine_b = lax.all_gather(summed, "rep", axis=0, tiled=False)

    vals = mine_b.reshape(n_rep, nb, j_slab, i_per, width).transpose(0, 3, 4, 2, 1)
    vals = vals.reshape(i_slab, width, j_slab, nb)
    my_b_lab = lax.dynamic_slice_in_dim(virt_irrep, dev_index * nb, nb)
    out = jnp.zeros((i_slab, v_width, j_slab, nb), jnp.float32)
    for p in range(parts_in(nb, v_width)):
        lab = my_b_lab[0] + p
        part = jnp.where((my_b_lab == lab)[None, None, None, :], vals, 0.0)
        start = wins[jnp.minimum(lab, N_IRREPS - 1)]
        placed = lax.dynamic_update_slice(
            jnp.zeros((i_slab, v_width, j_slab, nb), jnp.float32), part, (0, start, 0, 0)
        )
        out = out + placed
    return out


def solution(mesh):
    placed = (P(None, ("redist", "rep"), None, None), P(None, "redist", None, None), P(), P())
    return jax.shard_map(
        body, mesh=mesh, in_specs=placed, out_specs=P(None, None, None, "redist"), check_vma=False
    )
```

```python
import jax
import jax.numpy as jnp
from jax import lax
from jax.sharding import PartitionSpec as P

N_IRREPS = 8


def irrep_windows(virt_irrep, width):
    count = virt_irrep.shape[0]
    starts = jnp.sum(
        (virt_irrep[None, :] < jnp.arange(N_IRREPS, dtype=virt_irrep.dtype)[:, None]).astype(jnp.int32),
        axis=1,
    )
    return jnp.minimum(starts, count - width)


def parts_in(span, count):
    return min(N_IRREPS, -(-span // (count // 16)) + 1)


def shifted_pick(array, axis, width, wins, choice):
    out = None
    for g in range(N_IRREPS):
        cut = lax.dynamic_slice_in_dim(array, wins[g], width, axis=axis)
        out = cut if out is None else jnp.where(choice == g, cut, out)
    return out


def body(amplitudes, integrals, occ_irrep, virt_irrep):
    n_redist = lax.axis_size("redist")
    n_rep = lax.axis_size("rep")
    dev_index = lax.axis_index("redist")
    rep_index = lax.axis_index("rep")
    i_slab, k_block, v_width, _ = amplitudes.shape
    c_block = integrals.shape[1]
    j_slab = integrals.shape[2]
    if k_block != 1 or i_slab % n_rep:
        raise ValueError("unsupported split")
    i_per = i_slab // n_rep
    width = 3 * v_width // 16
    wins = irrep_windows(virt_irrep, width)
    occ_rows = occ_irrep[:i_slab]
    occ_js = occ_irrep[:j_slab]
    zero_bf = jnp.zeros((), amplitudes.dtype)

    my_k = dev_index * n_rep + rep_index
    my_lab = occ_irrep[my_k]
    a_win = jnp.bitwise_xor(virt_irrep, my_lab)
    amp = amplitudes[:, 0]
    amp_c = shifted_pick(amp, 2, width, wins, a_win[None, :, None])
    c_lab = shifted_pick(
        jnp.broadcast_to(virt_irrep[None, :], (v_width, v_width)), 1, width, wins, a_win[:, None]
    )
    allowed = jnp.bitwise_xor(occ_rows, my_lab)[:, None, None] == jnp.bitwise_xor(
        virt_irrep[:, None], c_lab
    )[None]
    amp_c = jnp.where(allowed, amp_c, zero_bf)
    amp_c = amp_c.reshape(n_rep, i_per, v_width, width)
    amp_g = lax.all_to_all(amp_c, "rep", split_axis=0, concat_axis=0, tiled=True)

    all_k_lab = occ_irrep[: integrals.shape[0]]
    my_c_lab = lax.dynamic_slice_in_dim(virt_irrep, dev_index * c_block, c_block)
    b_win = jnp.bitwise_xor(all_k_lab[:, None], my_c_lab[None, :])
    ints_t = jnp.transpose(integrals, (0, 2, 1, 3))
    ints_c = shifted_pick(ints_t, 3, width, wins, b_win[:, None, :, None])
    b_lab = shifted_pick(
        jnp.broadcast_to(virt_irrep, b_win.shape + (v_width,)), 2, width, wins, b_win[:, :, None]
    )
    sym = jnp.bitwise_xor(all_k_lab[:, None], my_c_lab[None, :])[:, None, :, None] == jnp.bitwise_xor(
        occ_js[None, :, None, None], b_lab[:, None, :, :]
    )
    ints_c = jnp.where(sym, ints_c, zero_bf)
    ints_c = ints_c.reshape(n_redist, n_rep, j_slab, c_block, width)
    ints_g = lax.all_to_all(ints_c, "redist", split_axis=0, concat_axis=3, tiled=True)[0]

    group_lab = occ_irrep[dev_index * n_rep + jnp.arange(n_rep, dtype=jnp.int32)]
    per_g = []
    for g in range(N_IRREPS):
        wa = wins[g]
        row_lab = lax.dynamic_slice_in_dim(virt_irrep, wa, width)
        a_parts = []
        i_parts = []
        for kk in range(n_rep):
            c_irrep = jnp.bitwise_xor(g, group_lab[kk])
            wc = wins[c_irrep]
            a_blk = lax.dynamic_slice_in_dim(amp_g[kk], wa, width, axis=1)
            a_parts.append(jnp.where((row_lab == g)[None, :, None], a_blk, zero_bf))
            cw_lab = lax.dynamic_slice_in_dim(virt_irrep, wc, width)
            i_blk = lax.dynamic_slice_in_dim(ints_g[kk], wc, width, axis=1)
            i_parts.append(jnp.where((cw_lab == c_irrep)[None, :, None], i_blk, zero_bf))
        a_cat = jnp.concatenate(a_parts, axis=2)
        i_cat = jnp.concatenate(i_parts, axis=1)
        blk = lax.dot_general(
            i_cat, a_cat, (((1,), (2,)), ((), ())), preferred_element_type=jnp.float32
        )
        per_g.append(jnp.transpose(blk, (1, 0, 2, 3)).reshape(width, -1))
    every = jnp.concatenate(per_g, axis=0)
    b_pos = jnp.arange(v_width, dtype=jnp.int32)
    pick = virt_irrep * width + (b_pos - wins[virt_irrep])
    compact = jnp.take(every, pick, axis=0)

    nb = v_width // n_redist
    pieces = lax.all_to_all(compact.reshape(n_redist, nb, -1), "redist", 0, 0, tiled=True)
    summed = jnp.sum(pieces, axis=0)
    mine_b = lax.all_gather(summed, "rep", axis=0, tiled=False)

    vals = mine_b.reshape(n_rep, nb, j_slab, i_per, width).transpose(0, 3, 4, 2, 1)
    vals = vals.reshape(i_slab, width, j_slab, nb)
    my_b_lab = lax.dynamic_slice_in_dim(virt_irrep, dev_index * nb, nb)
    padded = jnp.pad(vals, ((0, 0), (v_width, v_width - width), (0, 0), (0, 0)))
    out = None
    for p in range(parts_in(nb, v_width)):
        lab = my_b_lab[0] + p
        start = v_width - wins[jnp.minimum(lab, N_IRREPS - 1)]
        cut = lax.dynamic_slice_in_dim(padded, start, v_width, axis=1)
        out = cut if out is None else jnp.where((my_b_lab == lab)[None, None, None, :], cut, out)
    return out


def solution(mesh):
    placed = (P(None, ("redist", "rep"), None, None), P(None, "redist", None, None), P(), P())
    return jax.shard_map(
        body, mesh=mesh, in_specs=placed, out_specs=P(None, None, None, "redist"), check_vma=False
    )
```

```python
import jax
import jax.numpy as jnp
from jax import lax
from jax.sharding import PartitionSpec as P

N_IRREPS = 8


def irrep_windows(virt_irrep, width):
    count = virt_irrep.shape[0]
    starts = jnp.sum(
        (virt_irrep[None, :] < jnp.arange(N_IRREPS, dtype=virt_irrep.dtype)[:, None]).astype(jnp.int32),
        axis=1,
    )
    return jnp.minimum(starts, count - width)


def parts_in(span, count):
    return min(N_IRREPS, -(-span // (count // 16)) + 1)


def shifted_pick(array, axis, width, wins, choice):
    out = None
    for g in range(N_IRREPS):
        cut = lax.dynamic_slice_in_dim(array, wins[g], width, axis=axis)
        out = cut if out is None else jnp.where(choice == g, cut, out)
    return out


def body(amplitudes, integrals, occ_irrep, virt_irrep):
    n_redist = lax.axis_size("redist")
    n_rep = lax.axis_size("rep")
    dev_index = lax.axis_index("redist")
    rep_index = lax.axis_index("rep")
    i_slab, k_block, v_width, _ = amplitudes.shape
    c_block = integrals.shape[1]
    j_slab = integrals.shape[2]
    if k_block != 1:
        raise ValueError("unsupported split")
    width = 3 * v_width // 16
    wins = irrep_windows(virt_irrep, width)
    occ_rows = occ_irrep[:i_slab]
    occ_js = occ_irrep[:j_slab]
    zero_bf = jnp.zeros((), amplitudes.dtype)

    grouped = integrals.reshape(n_redist, n_rep, k_block, c_block, j_slab, v_width)
    ints_mine = lax.dynamic_slice_in_dim(grouped, rep_index, 1, 1).reshape(
        n_redist * k_block, c_block, j_slab, v_width
    )
    moved = lax.all_to_all(ints_mine, "redist", split_axis=0, concat_axis=1, tiled=True)[0]

    k_lab = occ_irrep[dev_index * n_rep + rep_index]
    amp = amplitudes[:, 0]
    pair_ik = jnp.bitwise_xor(occ_rows, k_lab)
    per_g = []
    for g in range(N_IRREPS):
        c_irrep = jnp.bitwise_xor(g, k_lab)
        wa = wins[g]
        wc = wins[c_irrep]
        a_lab = lax.dynamic_slice_in_dim(virt_irrep, wa, width)
        cw_lab = lax.dynamic_slice_in_dim(virt_irrep, wc, width)
        a_blk = lax.dynamic_slice(amp, (0, wa, wc), (i_slab, width, width))
        allowed = pair_ik[:, None, None] == jnp.bitwise_xor(a_lab[:, None], cw_lab[None, :])[None]
        a_blk = jnp.where(allowed, a_blk, zero_bf)
        i_blk = lax.dynamic_slice(moved, (wc, 0, wa), (width, j_slab, width))
        sym = (cw_lab == c_irrep)[:, None, None] & (
            jnp.bitwise_xor(cw_lab, k_lab)[:, None, None]
            == jnp.bitwise_xor(occ_js[:, None], a_lab[None, :])[None]
        )
        i_blk = jnp.where(sym, i_blk, zero_bf)
        blk = lax.dot_general(
            i_blk, a_blk, (((0,), (2,)), ((), ())), preferred_element_type=jnp.float32
        )
        per_g.append(jnp.transpose(blk, (1, 0, 2, 3)).reshape(width, -1))
    every = jnp.concatenate(per_g, axis=0)
    b_pos = jnp.arange(v_width, dtype=jnp.int32)
    pick = virt_irrep * width + (b_pos - wins[virt_irrep])
    compact = jnp.take(every, pick, axis=0)

    n_all = n_redist * n_rep
    nb_all = v_width // n_all
    pieces = lax.all_to_all(compact.reshape(n_all, nb_all, -1), ("redist", "rep"), 0, 0, tiled=True)
    summed = jnp.sum(pieces, axis=0)
    mine_b = lax.all_gather(summed, "rep", axis=0, tiled=True)

    nb = mine_b.shape[0]
    vals = mine_b.reshape(nb, j_slab, i_slab, width).transpose(2, 3, 1, 0)
    my_b_lab = lax.dynamic_slice_in_dim(virt_irrep, dev_index * nb, nb)
    padded = jnp.pad(vals, ((0, 0), (v_width, v_width - width), (0, 0), (0, 0)))
    out = None
    for p in range(parts_in(nb, v_width)):
        lab = my_b_lab[0] + p
        start = v_width - wins[jnp.minimum(lab, N_IRREPS - 1)]
        cut = lax.dynamic_slice_in_dim(padded, start, v_width, axis=1)
        out = cut if out is None else jnp.where((my_b_lab == lab)[None, None, None, :], cut, out)
    return out


def solution(mesh):
    placed = (P(None, ("redist", "rep"), None, None), P(None, "redist", None, None), P(), P())
    return jax.shard_map(
        body, mesh=mesh, in_specs=placed, out_specs=P(None, None, None, "redist"), check_vma=False
    )
```

```python
import jax
import jax.numpy as jnp
from jax import lax
from jax.sharding import PartitionSpec as P

N_IRREPS = 8


def irrep_windows(virt_irrep, width):
    count = virt_irrep.shape[0]
    starts = jnp.sum(
        (virt_irrep[None, :] < jnp.arange(N_IRREPS, dtype=virt_irrep.dtype)[:, None]).astype(jnp.int32),
        axis=1,
    )
    return jnp.minimum(starts, count - width)


def parts_in(span, count):
    return min(N_IRREPS, -(-span // (count // 16)) + 1)


def shifted_pick(array, axis, width, wins, choice):
    out = None
    for g in range(N_IRREPS):
        cut = lax.dynamic_slice_in_dim(array, wins[g], width, axis=axis)
        out = cut if out is None else jnp.where(choice == g, cut, out)
    return out


def body(amplitudes, integrals, occ_irrep, virt_irrep):
    n_redist = lax.axis_size("redist")
    n_rep = lax.axis_size("rep")
    dev_index = lax.axis_index("redist")
    rep_index = lax.axis_index("rep")
    i_slab, k_block, v_width, _ = amplitudes.shape
    c_block = integrals.shape[1]
    j_slab = integrals.shape[2]
    if k_block != 1:
        raise ValueError("unsupported split")
    width = 3 * v_width // 16
    wins = irrep_windows(virt_irrep, width)
    occ_rows = occ_irrep[:i_slab]
    occ_js = occ_irrep[:j_slab]
    zero_bf = jnp.zeros((), amplitudes.dtype)

    grouped = integrals.reshape(n_redist, n_rep, k_block, c_block, j_slab, v_width)
    ints_mine = lax.dynamic_slice_in_dim(grouped, rep_index, 1, 1).reshape(
        n_redist * k_block, c_block, j_slab, v_width
    )

    k_lab = occ_irrep[dev_index * n_rep + rep_index]
    amp = amplitudes[:, 0]
    pair_ik = jnp.bitwise_xor(occ_rows, k_lab)
    a_blks = []
    for g in range(N_IRREPS):
        wa = wins[g]
        wc = wins[jnp.bitwise_xor(g, k_lab)]
        a_lab = lax.dynamic_slice_in_dim(virt_irrep, wa, width)
        cw_lab = lax.dynamic_slice_in_dim(virt_irrep, wc, width)
        a_blk = lax.dynamic_slice(amp, (0, wa, wc), (i_slab, width, width))
        allowed = pair_ik[:, None, None] == jnp.bitwise_xor(a_lab[:, None], cw_lab[None, :])[None]
        a_blks.append(jnp.where(allowed, a_blk, zero_bf))

    b_pos = jnp.arange(v_width, dtype=jnp.int32)
    pick = virt_irrep * width + (b_pos - wins[virt_irrep])
    n_all = n_redist * n_rep
    nb_all = v_width // n_all
    per_j = []
    for jj in range(j_slab):
        moved = lax.all_to_all(
            ints_mine[:, :, jj], "redist", split_axis=0, concat_axis=1, tiled=True
        )[0]
        per_g = []
        for g in range(N_IRREPS):
            c_irrep = jnp.bitwise_xor(g, k_lab)
            wa = wins[g]
            wc = wins[c_irrep]
            a_lab = lax.dynamic_slice_in_dim(virt_irrep, wa, width)
            cw_lab = lax.dynamic_slice_in_dim(virt_irrep, wc, width)
            i_blk = lax.dynamic_slice(moved, (wc, wa), (width, width))
            sym = (cw_lab == c_irrep)[:, None] & (
                jnp.bitwise_xor(cw_lab, k_lab)[:, None] == jnp.bitwise_xor(occ_js[jj], a_lab)[None, :]
            )
            i_blk = jnp.where(sym, i_blk, zero_bf)
            blk = lax.dot_general(
                i_blk, a_blks[g], (((0,), (2,)), ((), ())), preferred_element_type=jnp.float32
            )
            per_g.append(blk.reshape(width, -1))
        every = jnp.concatenate(per_g, axis=0)
        compact = jnp.take(every, pick, axis=0)
        pieces = lax.all_to_all(
            compact.reshape(n_all, nb_all, -1), ("redist", "rep"), 0, 0, tiled=True
        )
        summed = jnp.sum(pieces, axis=0)
        per_j.append(lax.all_gather(summed, "rep", axis=0, tiled=True))
    mine_b = jnp.stack(per_j, axis=1)

    nb = mine_b.shape[0]
    vals = mine_b.reshape(nb, j_slab, i_slab, width).transpose(2, 3, 1, 0)
    my_b_lab = lax.dynamic_slice_in_dim(virt_irrep, dev_index * nb, nb)
    padded = jnp.pad(vals, ((0, 0), (v_width, v_width - width), (0, 0), (0, 0)))
    out = None
    for p in range(parts_in(nb, v_width)):
        lab = my_b_lab[0] + p
        start = v_width - wins[jnp.minimum(lab, N_IRREPS - 1)]
        cut = lax.dynamic_slice_in_dim(padded, start, v_width, axis=1)
        out = cut if out is None else jnp.where((my_b_lab == lab)[None, None, None, :], cut, out)
    return out


def solution(mesh):
    placed = (P(None, ("redist", "rep"), None, None), P(None, "redist", None, None), P(), P())
    return jax.shard_map(
        body, mesh=mesh, in_specs=placed, out_specs=P(None, None, None, "redist"), check_vma=False
    )
```

```python
import jax
import jax.numpy as jnp
from jax import lax
from jax.sharding import PartitionSpec as P

N_IRREPS = 8


def irrep_windows(virt_irrep, width):
    count = virt_irrep.shape[0]
    starts = jnp.sum(
        (virt_irrep[None, :] < jnp.arange(N_IRREPS, dtype=virt_irrep.dtype)[:, None]).astype(jnp.int32),
        axis=1,
    )
    return jnp.minimum(starts, count - width)


def parts_in(span, count):
    return min(N_IRREPS, -(-span // (count // 16)) + 1)


def shifted_pick(array, axis, width, wins, choice):
    out = None
    for g in range(N_IRREPS):
        cut = lax.dynamic_slice_in_dim(array, wins[g], width, axis=axis)
        out = cut if out is None else jnp.where(choice == g, cut, out)
    return out


def body(amplitudes, integrals, occ_irrep, virt_irrep):
    n_redist = lax.axis_size("redist")
    n_rep = lax.axis_size("rep")
    dev_index = lax.axis_index("redist")
    rep_index = lax.axis_index("rep")
    i_slab, k_block, v_width, _ = amplitudes.shape
    c_block = integrals.shape[1]
    j_slab = integrals.shape[2]
    if k_block != 1:
        raise ValueError("unsupported split")
    width = 3 * v_width // 16
    wins = irrep_windows(virt_irrep, width)
    occ_rows = occ_irrep[:i_slab]
    occ_js = occ_irrep[:j_slab]
    zero_bf = jnp.zeros((), amplitudes.dtype)

    grouped = integrals.reshape(n_redist, n_rep, k_block, c_block, j_slab, v_width)
    ints_mine = lax.dynamic_slice_in_dim(grouped, rep_index, 1, 1).reshape(
        n_redist * k_block, c_block, j_slab, v_width
    )
    moved = lax.all_to_all(ints_mine, "redist", split_axis=0, concat_axis=1, tiled=True)[0]

    k_lab = occ_irrep[dev_index * n_rep + rep_index]
    amp = amplitudes[:, 0]
    pair_ik = jnp.bitwise_xor(occ_rows, k_lab)
    a_blks = []
    for g in range(N_IRREPS):
        wa = wins[g]
        wc = wins[jnp.bitwise_xor(g, k_lab)]
        a_lab = lax.dynamic_slice_in_dim(virt_irrep, wa, width)
        cw_lab = lax.dynamic_slice_in_dim(virt_irrep, wc, width)
        a_blk = lax.dynamic_slice(amp, (0, wa, wc), (i_slab, width, width))
        allowed = pair_ik[:, None, None] == jnp.bitwise_xor(a_lab[:, None], cw_lab[None, :])[None]
        a_blks.append(jnp.where(allowed, a_blk, zero_bf))
    a_blks = lax.optimization_barrier(jnp.stack(a_blks))
    per_g = []
    for g in range(N_IRREPS):
        c_irrep = jnp.bitwise_xor(g, k_lab)
        wa = wins[g]
        wc = wins[c_irrep]
        a_lab = lax.dynamic_slice_in_dim(virt_irrep, wa, width)
        cw_lab = lax.dynamic_slice_in_dim(virt_irrep, wc, width)
        i_blk = lax.dynamic_slice(moved, (wc, 0, wa), (width, j_slab, width))
        sym = (cw_lab == c_irrep)[:, None, None] & (
            jnp.bitwise_xor(cw_lab, k_lab)[:, None, None]
            == jnp.bitwise_xor(occ_js[:, None], a_lab[None, :])[None]
        )
        i_blk = jnp.where(sym, i_blk, zero_bf)
        blk = lax.dot_general(
            i_blk, a_blks[g], (((0,), (2,)), ((), ())), preferred_element_type=jnp.float32
        )
        per_g.append(jnp.transpose(blk, (1, 0, 2, 3)).reshape(width, -1))
    every = jnp.concatenate(per_g, axis=0)
    b_pos = jnp.arange(v_width, dtype=jnp.int32)
    pick = virt_irrep * width + (b_pos - wins[virt_irrep])
    compact = jnp.take(every, pick, axis=0)

    n_all = n_redist * n_rep
    nb_all = v_width // n_all
    pieces = lax.all_to_all(compact.reshape(n_all, nb_all, -1), ("redist", "rep"), 0, 0, tiled=True)
    summed = jnp.sum(pieces, axis=0)
    mine_b = lax.all_gather(summed, "rep", axis=0, tiled=True)

    nb = mine_b.shape[0]
    vals = mine_b.reshape(nb, j_slab, i_slab, width).transpose(2, 3, 1, 0)
    my_b_lab = lax.dynamic_slice_in_dim(virt_irrep, dev_index * nb, nb)
    padded = jnp.pad(vals, ((0, 0), (v_width, v_width - width), (0, 0), (0, 0)))
    out = None
    for p in range(parts_in(nb, v_width)):
        lab = my_b_lab[0] + p
        start = v_width - wins[jnp.minimum(lab, N_IRREPS - 1)]
        cut = lax.dynamic_slice_in_dim(padded, start, v_width, axis=1)
        out = cut if out is None else jnp.where((my_b_lab == lab)[None, None, None, :], cut, out)
    return out


def solution(mesh):
    placed = (P(None, ("redist", "rep"), None, None), P(None, "redist", None, None), P(), P())
    return jax.shard_map(
        body, mesh=mesh, in_specs=placed, out_specs=P(None, None, None, "redist"), check_vma=False
    )
```

```python
import jax
import jax.numpy as jnp
from jax import lax
from jax.sharding import PartitionSpec as P

N_IRREPS = 8


def irrep_windows(virt_irrep, width):
    count = virt_irrep.shape[0]
    starts = jnp.sum(
        (virt_irrep[None, :] < jnp.arange(N_IRREPS, dtype=virt_irrep.dtype)[:, None]).astype(jnp.int32),
        axis=1,
    )
    return jnp.minimum(starts, count - width)


def parts_in(span, count):
    return min(N_IRREPS, -(-span // (count // 16)) + 1)


def shifted_pick(array, axis, width, wins, choice):
    out = None
    for g in range(N_IRREPS):
        cut = lax.dynamic_slice_in_dim(array, wins[g], width, axis=axis)
        out = cut if out is None else jnp.where(choice == g, cut, out)
    return out


def body(amplitudes, integrals, occ_irrep, virt_irrep):
    n_redist = lax.axis_size("redist")
    n_rep = lax.axis_size("rep")
    dev_index = lax.axis_index("redist")
    rep_index = lax.axis_index("rep")
    i_slab, k_block, v_width, _ = amplitudes.shape
    c_block = integrals.shape[1]
    j_slab = integrals.shape[2]
    if k_block != 1:
        raise ValueError("unsupported split")
    width = 3 * v_width // 16
    wins = irrep_windows(virt_irrep, width)
    occ_rows = occ_irrep[:i_slab]
    occ_js = occ_irrep[:j_slab]
    zero_bf = jnp.zeros((), amplitudes.dtype)

    grouped = integrals.reshape(n_redist, n_rep, k_block, c_block, j_slab, v_width)
    ints_mine = lax.dynamic_slice_in_dim(grouped, rep_index, 1, 1).reshape(
        n_redist * k_block, c_block, j_slab, v_width
    )
    moved = lax.all_to_all(ints_mine, "redist", split_axis=0, concat_axis=1, tiled=True)[0]

    k_lab = occ_irrep[dev_index * n_rep + rep_index]
    amp = amplitudes[:, 0]
    pair_ik = jnp.bitwise_xor(occ_rows, k_lab)
    per_g = []
    for g in range(N_IRREPS):
        c_irrep = jnp.bitwise_xor(g, k_lab)
        wa = wins[g]
        wc = wins[c_irrep]
        a_lab = lax.dynamic_slice_in_dim(virt_irrep, wa, width)
        cw_lab = lax.dynamic_slice_in_dim(virt_irrep, wc, width)
        a_blk = lax.dynamic_slice(amp, (0, wa, wc), (i_slab, width, width))
        allowed = pair_ik[:, None, None] == jnp.bitwise_xor(a_lab[:, None], cw_lab[None, :])[None]
        a_blk = jnp.where(allowed, a_blk, zero_bf)
        i_blk = lax.dynamic_slice(moved, (wc, 0, wa), (width, j_slab, width))
        sym = (cw_lab == c_irrep)[:, None, None] & (
            jnp.bitwise_xor(cw_lab, k_lab)[:, None, None]
            == jnp.bitwise_xor(occ_js[:, None], a_lab[None, :])[None]
        )
        i_blk = jnp.where(sym, i_blk, zero_bf)
        blk = lax.dot_general(
            jnp.transpose(i_blk, (2, 1, 0)), a_blk, (((2,), (2,)), ((), ())),
            preferred_element_type=jnp.float32,
        )
        per_g.append(blk.reshape(width, -1))
    every = jnp.concatenate(per_g, axis=0)
    b_pos = jnp.arange(v_width, dtype=jnp.int32)
    pick = virt_irrep * width + (b_pos - wins[virt_irrep])
    compact = jnp.take(every, pick, axis=0, mode="clip")

    n_all = n_redist * n_rep
    nb_all = v_width // n_all
    pieces = lax.all_to_all(compact.reshape(n_all, nb_all, -1), ("redist", "rep"), 0, 0, tiled=True)
    summed = jnp.sum(pieces, axis=0)
    mine_b = lax.all_gather(summed, "rep", axis=0, tiled=True)

    nb = mine_b.shape[0]
    vals = mine_b.reshape(nb, j_slab, i_slab, width).transpose(2, 3, 1, 0)
    my_b_lab = lax.dynamic_slice_in_dim(virt_irrep, dev_index * nb, nb)
    padded = jnp.pad(vals, ((0, 0), (v_width, v_width - width), (0, 0), (0, 0)))
    out = None
    for p in range(parts_in(nb, v_width)):
        lab = my_b_lab[0] + p
        start = v_width - wins[jnp.minimum(lab, N_IRREPS - 1)]
        cut = lax.dynamic_slice_in_dim(padded, start, v_width, axis=1)
        out = cut if out is None else jnp.where((my_b_lab == lab)[None, None, None, :], cut, out)
    return out


def solution(mesh):
    placed = (P(None, ("redist", "rep"), None, None), P(None, "redist", None, None), P(), P())
    return jax.shard_map(
        body, mesh=mesh, in_specs=placed, out_specs=P(None, None, None, "redist"), check_vma=False
    )
```

```python
import jax
import jax.numpy as jnp
from jax import lax
from jax.sharding import PartitionSpec as P

N_IRREPS = 8


def irrep_windows(virt_irrep, width):
    count = virt_irrep.shape[0]
    starts = jnp.sum(
        (virt_irrep[None, :] < jnp.arange(N_IRREPS, dtype=virt_irrep.dtype)[:, None]).astype(jnp.int32),
        axis=1,
    )
    return jnp.minimum(starts, count - width)


def parts_in(span, count):
    return min(N_IRREPS, -(-span // (count // 16)) + 1)


def shifted_pick(array, axis, width, wins, choice):
    out = None
    for g in range(N_IRREPS):
        cut = lax.dynamic_slice_in_dim(array, wins[g], width, axis=axis)
        out = cut if out is None else jnp.where(choice == g, cut, out)
    return out


def body(amplitudes, integrals, occ_irrep, virt_irrep):
    n_redist = lax.axis_size("redist")
    n_rep = lax.axis_size("rep")
    dev_index = lax.axis_index("redist")
    rep_index = lax.axis_index("rep")
    i_slab, k_block, v_width, _ = amplitudes.shape
    c_block = integrals.shape[1]
    j_slab = integrals.shape[2]
    if k_block != 1:
        raise ValueError("unsupported split")
    width = 3 * v_width // 16
    wins = irrep_windows(virt_irrep, width)
    occ_rows = occ_irrep[:i_slab]
    occ_js = occ_irrep[:j_slab]
    zero_bf = jnp.zeros((), amplitudes.dtype)

    grouped = integrals.reshape(n_redist, n_rep, k_block, c_block, j_slab, v_width)
    ints_mine = lax.dynamic_slice_in_dim(grouped, rep_index, 1, 1).reshape(
        n_redist * k_block, c_block, j_slab, v_width
    )
    dest_lab = occ_irrep[jnp.arange(n_redist, dtype=jnp.int32) * n_rep + rep_index]
    my_c_lab = lax.dynamic_slice_in_dim(virt_irrep, dev_index * c_block, c_block)
    b_win = jnp.bitwise_xor(dest_lab[:, None], my_c_lab[None, :])
    packed = shifted_pick(ints_mine, 3, width, wins, b_win[:, :, None, None])
    moved = lax.all_to_all(packed, "redist", split_axis=0, concat_axis=1, tiled=True)[0]

    k_lab = occ_irrep[dev_index * n_rep + rep_index]
    amp = amplitudes[:, 0]
    pair_ik = jnp.bitwise_xor(occ_rows, k_lab)
    per_g = []
    for g in range(N_IRREPS):
        c_irrep = jnp.bitwise_xor(g, k_lab)
        wa = wins[g]
        wc = wins[c_irrep]
        a_lab = lax.dynamic_slice_in_dim(virt_irrep, wa, width)
        cw_lab = lax.dynamic_slice_in_dim(virt_irrep, wc, width)
        a_blk = lax.dynamic_slice(amp, (0, wa, wc), (i_slab, width, width))
        allowed = pair_ik[:, None, None] == jnp.bitwise_xor(a_lab[:, None], cw_lab[None, :])[None]
        a_blk = jnp.where(allowed, a_blk, zero_bf)
        i_blk = lax.dynamic_slice(moved, (wc, 0, 0), (width, j_slab, width))
        sym = (cw_lab == c_irrep)[:, None, None] & (
            jnp.bitwise_xor(cw_lab, k_lab)[:, None, None]
            == jnp.bitwise_xor(occ_js[:, None], a_lab[None, :])[None]
        )
        i_blk = jnp.where(sym, i_blk, zero_bf)
        blk = lax.dot_general(
            jnp.transpose(i_blk, (2, 1, 0)), a_blk, (((2,), (2,)), ((), ())),
            preferred_element_type=jnp.float32,
        )
        per_g.append(blk.reshape(width, -1))
    every = jnp.concatenate(per_g, axis=0)
    b_pos = jnp.arange(v_width, dtype=jnp.int32)
    pick = virt_irrep * width + (b_pos - wins[virt_irrep])
    compact = jnp.take(every, pick, axis=0, mode="clip")

    n_all = n_redist * n_rep
    nb_all = v_width // n_all
    pieces = lax.all_to_all(compact.reshape(n_all, nb_all, -1), ("redist", "rep"), 0, 0, tiled=True)
    summed = jnp.sum(pieces, axis=0)
    mine_b = lax.all_gather(summed, "rep", axis=0, tiled=True)

    nb = mine_b.shape[0]
    vals = mine_b.reshape(nb, j_slab, i_slab, width).transpose(2, 3, 1, 0)
    my_b_lab = lax.dynamic_slice_in_dim(virt_irrep, dev_index * nb, nb)
    padded = jnp.pad(vals, ((0, 0), (v_width, v_width - width), (0, 0), (0, 0)))
    out = None
    for p in range(parts_in(nb, v_width)):
        lab = my_b_lab[0] + p
        start = v_width - wins[jnp.minimum(lab, N_IRREPS - 1)]
        cut = lax.dynamic_slice_in_dim(padded, start, v_width, axis=1)
        out = cut if out is None else jnp.where((my_b_lab == lab)[None, None, None, :], cut, out)
    return out


def solution(mesh):
    placed = (P(None, ("redist", "rep"), None, None), P(None, "redist", None, None), P(), P())
    return jax.shard_map(
        body, mesh=mesh, in_specs=placed, out_specs=P(None, None, None, "redist"), check_vma=False
    )
```

```python
import jax
import jax.numpy as jnp
from jax import lax
from jax.sharding import PartitionSpec as P

N_IRREPS = 8


def irrep_windows(virt_irrep, width):
    count = virt_irrep.shape[0]
    starts = jnp.sum(
        (virt_irrep[None, :] < jnp.arange(N_IRREPS, dtype=virt_irrep.dtype)[:, None]).astype(jnp.int32),
        axis=1,
    )
    return jnp.minimum(starts, count - width)


def parts_in(span, count):
    return min(N_IRREPS, -(-span // (count // 16)) + 1)


def shifted_pick(array, axis, width, wins, choice):
    out = None
    for g in range(N_IRREPS):
        cut = lax.dynamic_slice_in_dim(array, wins[g], width, axis=axis)
        out = cut if out is None else jnp.where(choice == g, cut, out)
    return out


def body(amplitudes, integrals, occ_irrep, virt_irrep):
    n_redist = lax.axis_size("redist")
    n_rep = lax.axis_size("rep")
    dev_index = lax.axis_index("redist")
    rep_index = lax.axis_index("rep")
    i_slab, k_block, v_width, _ = amplitudes.shape
    c_block = integrals.shape[1]
    j_slab = integrals.shape[2]
    if k_block != 1:
        raise ValueError("unsupported split")
    width = 3 * v_width // 16
    wins = irrep_windows(virt_irrep, width)
    occ_rows = occ_irrep[:i_slab]
    occ_js = occ_irrep[:j_slab]
    zero_bf = jnp.zeros((), amplitudes.dtype)

    grouped = integrals.reshape(n_redist, n_rep, k_block, c_block, j_slab, v_width)
    ints_mine = lax.dynamic_slice_in_dim(grouped, rep_index, 1, 1).reshape(
        n_redist * k_block, c_block, j_slab, v_width
    )
    dest_lab = lax.dynamic_index_in_dim(
        occ_irrep[: n_redist * n_rep].reshape(n_redist, n_rep), rep_index, 1, keepdims=False
    )
    my_c_lab = lax.dynamic_slice_in_dim(virt_irrep, dev_index * c_block, c_block)
    b_win = jnp.bitwise_xor(dest_lab[:, None], my_c_lab[None, :])
    packed = shifted_pick(ints_mine, 3, width, wins, b_win[:, :, None, None])
    moved = lax.all_to_all(packed, "redist", split_axis=0, concat_axis=1, tiled=True)[0]

    k_lab = occ_irrep[dev_index * n_rep + rep_index]
    amp = amplitudes[:, 0]
    pair_ik = jnp.bitwise_xor(occ_rows, k_lab)
    per_g = []
    for g in range(N_IRREPS):
        c_irrep = jnp.bitwise_xor(g, k_lab)
        wa = wins[g]
        wc = wins[c_irrep]
        a_lab = lax.dynamic_slice_in_dim(virt_irrep, wa, width)
        cw_lab = lax.dynamic_slice_in_dim(virt_irrep, wc, width)
        a_blk = lax.dynamic_slice(amp, (0, wa, wc), (i_slab, width, width))
        allowed = pair_ik[:, None, None] == jnp.bitwise_xor(a_lab[:, None], cw_lab[None, :])[None]
        a_blk = jnp.where(allowed, a_blk, zero_bf)
        i_blk = lax.dynamic_slice(moved, (wc, 0, 0), (width, j_slab, width))
        sym = (cw_lab == c_irrep)[:, None, None] & (
            jnp.bitwise_xor(cw_lab, k_lab)[:, None, None]
            == jnp.bitwise_xor(occ_js[:, None], a_lab[None, :])[None]
        )
        i_blk = jnp.where(sym, i_blk, zero_bf)
        blk = lax.dot_general(
            jnp.transpose(i_blk, (2, 1, 0)), a_blk, (((2,), (2,)), ((), ())),
            preferred_element_type=jnp.float32,
        )
        per_g.append(blk.reshape(width, -1))
    every = jnp.concatenate(per_g, axis=0)
    b_pos = jnp.arange(v_width, dtype=jnp.int32)
    b_win_start = jnp.zeros_like(virt_irrep)
    for g in range(N_IRREPS):
        b_win_start = jnp.where(virt_irrep == g, wins[g], b_win_start)
    pick = virt_irrep * width + (b_pos - b_win_start)
    compact = jnp.take(every, pick, axis=0, mode="clip")

    n_all = n_redist * n_rep
    nb_all = v_width // n_all
    pieces = lax.all_to_all(compact.reshape(n_all, nb_all, -1), ("redist", "rep"), 0, 0, tiled=True)
    summed = jnp.sum(pieces, axis=0)
    mine_b = lax.all_gather(summed, "rep", axis=0, tiled=True)

    nb = mine_b.shape[0]
    vals = mine_b.reshape(nb, j_slab, i_slab, width).transpose(2, 3, 1, 0)
    my_b_lab = lax.dynamic_slice_in_dim(virt_irrep, dev_index * nb, nb)
    padded = jnp.pad(vals, ((0, 0), (v_width, v_width - width), (0, 0), (0, 0)))
    out = None
    for p in range(parts_in(nb, v_width)):
        lab = my_b_lab[0] + p
        start = v_width - wins[jnp.minimum(lab, N_IRREPS - 1)]
        cut = lax.dynamic_slice_in_dim(padded, start, v_width, axis=1)
        out = cut if out is None else jnp.where((my_b_lab == lab)[None, None, None, :], cut, out)
    return out


def solution(mesh):
    placed = (P(None, ("redist", "rep"), None, None), P(None, "redist", None, None), P(), P())
    return jax.shard_map(
        body, mesh=mesh, in_specs=placed, out_specs=P(None, None, None, "redist"), check_vma=False
    )
```

```python
import jax
import jax.numpy as jnp
from jax import lax
from jax.sharding import PartitionSpec as P

N_IRREPS = 8


def irrep_windows(virt_irrep, width):
    count = virt_irrep.shape[0]
    starts = jnp.sum(
        (virt_irrep[None, :] < jnp.arange(N_IRREPS, dtype=virt_irrep.dtype)[:, None]).astype(jnp.int32),
        axis=1,
    )
    return jnp.minimum(starts, count - width)


def parts_in(span, count):
    return min(N_IRREPS, -(-span // (count // 16)) + 1)


def shifted_pick(array, axis, width, wins, choice):
    out = None
    for g in range(N_IRREPS):
        cut = lax.dynamic_slice_in_dim(array, wins[g], width, axis=axis)
        out = cut if out is None else jnp.where(choice == g, cut, out)
    return out


def body(amplitudes, integrals, occ_irrep, virt_irrep):
    n_redist = lax.axis_size("redist")
    n_rep = lax.axis_size("rep")
    dev_index = lax.axis_index("redist")
    rep_index = lax.axis_index("rep")
    i_slab, k_block, v_width, _ = amplitudes.shape
    c_block = integrals.shape[1]
    j_slab = integrals.shape[2]
    if k_block != 1:
        raise ValueError("unsupported split")
    width = 3 * v_width // 16
    wins = irrep_windows(virt_irrep, width)
    occ_rows = occ_irrep[:i_slab]
    occ_js = occ_irrep[:j_slab]
    zero_bf = jnp.zeros((), amplitudes.dtype)

    grouped = integrals.reshape(n_redist, n_rep, k_block, c_block, j_slab, v_width)
    ints_mine = lax.dynamic_slice_in_dim(grouped, rep_index, 1, 1).reshape(
        n_redist * k_block, c_block, j_slab, v_width
    )
    dest_lab = lax.dynamic_index_in_dim(
        occ_irrep[: n_redist * n_rep].reshape(n_redist, n_rep), rep_index, 1, keepdims=False
    )
    my_c_lab = lax.dynamic_slice_in_dim(virt_irrep, dev_index * c_block, c_block)
    b_win = jnp.bitwise_xor(dest_lab[:, None], my_c_lab[None, :])
    b_iota = jnp.arange(v_width, dtype=jnp.int32)
    t_iota = jnp.arange(width, dtype=jnp.int32)
    selector = (b_iota[None, :, None] == wins[:, None, None] + t_iota[None, None, :]).astype(
        integrals.dtype
    )
    every_win = lax.dot_general(
        ints_mine, selector, (((3,), (1,)), ((), ())), preferred_element_type=jnp.float32
    )
    packed = every_win[:, :, :, 0]
    for g in range(1, N_IRREPS):
        packed = jnp.where((b_win == g)[:, :, None, None], every_win[:, :, :, g], packed)
    packed = packed.astype(integrals.dtype)
    moved = lax.all_to_all(packed, "redist", split_axis=0, concat_axis=1, tiled=True)[0]

    k_lab = occ_irrep[dev_index * n_rep + rep_index]
    amp = amplitudes[:, 0]
    pair_ik = jnp.bitwise_xor(occ_rows, k_lab)
    per_g = []
    for g in range(N_IRREPS):
        c_irrep = jnp.bitwise_xor(g, k_lab)
        wa = wins[g]
        wc = wins[c_irrep]
        a_lab = lax.dynamic_slice_in_dim(virt_irrep, wa, width)
        cw_lab = lax.dynamic_slice_in_dim(virt_irrep, wc, width)
        a_blk = lax.dynamic_slice(amp, (0, wa, wc), (i_slab, width, width))
        allowed = pair_ik[:, None, None] == jnp.bitwise_xor(a_lab[:, None], cw_lab[None, :])[None]
        a_blk = jnp.where(allowed, a_blk, zero_bf)
        i_blk = lax.dynamic_slice(moved, (wc, 0, 0), (width, j_slab, width))
        sym = (cw_lab == c_irrep)[:, None, None] & (
            jnp.bitwise_xor(cw_lab, k_lab)[:, None, None]
            == jnp.bitwise_xor(occ_js[:, None], a_lab[None, :])[None]
        )
        i_blk = jnp.where(sym, i_blk, zero_bf)
        blk = lax.dot_general(
            jnp.transpose(i_blk, (2, 1, 0)), a_blk, (((2,), (2,)), ((), ())),
            preferred_element_type=jnp.float32,
        )
        per_g.append(blk.reshape(width, -1))
    every = jnp.concatenate(per_g, axis=0)
    b_pos = jnp.arange(v_width, dtype=jnp.int32)
    b_win_start = jnp.zeros_like(virt_irrep)
    for g in range(N_IRREPS):
        b_win_start = jnp.where(virt_irrep == g, wins[g], b_win_start)
    pick = virt_irrep * width + (b_pos - b_win_start)
    compact = jnp.take(every, pick, axis=0, mode="clip")

    n_all = n_redist * n_rep
    nb_all = v_width // n_all
    pieces = lax.all_to_all(compact.reshape(n_all, nb_all, -1), ("redist", "rep"), 0, 0, tiled=True)
    summed = jnp.sum(pieces, axis=0)
    mine_b = lax.all_gather(summed, "rep", axis=0, tiled=True)

    nb = mine_b.shape[0]
    vals = mine_b.reshape(nb, j_slab, i_slab, width).transpose(2, 3, 1, 0)
    my_b_lab = lax.dynamic_slice_in_dim(virt_irrep, dev_index * nb, nb)
    padded = jnp.pad(vals, ((0, 0), (v_width, v_width - width), (0, 0), (0, 0)))
    out = None
    for p in range(parts_in(nb, v_width)):
        lab = my_b_lab[0] + p
        start = v_width - wins[jnp.minimum(lab, N_IRREPS - 1)]
        cut = lax.dynamic_slice_in_dim(padded, start, v_width, axis=1)
        out = cut if out is None else jnp.where((my_b_lab == lab)[None, None, None, :], cut, out)
    return out


def solution(mesh):
    placed = (P(None, ("redist", "rep"), None, None), P(None, "redist", None, None), P(), P())
    return jax.shard_map(
        body, mesh=mesh, in_specs=placed, out_specs=P(None, None, None, "redist"), check_vma=False
    )
```

```python
import jax
import jax.numpy as jnp
from jax import lax
from jax.sharding import PartitionSpec as P

N_IRREPS = 8


def irrep_windows(virt_irrep, width):
    count = virt_irrep.shape[0]
    starts = jnp.sum(
        (virt_irrep[None, :] < jnp.arange(N_IRREPS, dtype=virt_irrep.dtype)[:, None]).astype(jnp.int32),
        axis=1,
    )
    return jnp.minimum(starts, count - width)


def parts_in(span, count):
    return min(N_IRREPS, -(-span // (count // 16)) + 1)


def shifted_pick(array, axis, width, wins, choice):
    out = None
    for g in range(N_IRREPS):
        cut = lax.dynamic_slice_in_dim(array, wins[g], width, axis=axis)
        out = cut if out is None else jnp.where(choice == g, cut, out)
    return out


def body(amplitudes, integrals, occ_irrep, virt_irrep):
    n_redist = lax.axis_size("redist")
    n_rep = lax.axis_size("rep")
    dev_index = lax.axis_index("redist")
    rep_index = lax.axis_index("rep")
    i_slab, k_block, v_width, _ = amplitudes.shape
    c_block = integrals.shape[1]
    j_slab = integrals.shape[2]
    if k_block != 1:
        raise ValueError("unsupported split")
    width = 3 * v_width // 16
    wins = irrep_windows(virt_irrep, width)
    occ_rows = occ_irrep[:i_slab]
    occ_js = occ_irrep[:j_slab]
    zero_bf = jnp.zeros((), amplitudes.dtype)

    grouped = integrals.reshape(n_redist, n_rep, k_block, c_block, j_slab, v_width)
    ints_mine = lax.dynamic_slice_in_dim(grouped, rep_index, 1, 1).reshape(
        n_redist * k_block, c_block, j_slab, v_width
    )
    dest_lab = lax.dynamic_index_in_dim(
        occ_irrep[: n_redist * n_rep].reshape(n_redist, n_rep), rep_index, 1, keepdims=False
    )
    my_c_lab = lax.dynamic_slice_in_dim(virt_irrep, dev_index * c_block, c_block)
    b_win = jnp.bitwise_xor(dest_lab[:, None], my_c_lab[None, :])
    b_iota = jnp.arange(v_width, dtype=jnp.int32)
    t_iota = jnp.arange(width, dtype=jnp.int32)
    selector = (b_iota[None, :, None] == wins[:, None, None] + t_iota[None, None, :]).astype(
        integrals.dtype
    )
    every_win = lax.dot_general(
        ints_mine, selector, (((3,), (1,)), ((), ())), preferred_element_type=jnp.float32
    )
    packed = every_win[:, :, :, 0]
    for g in range(1, N_IRREPS):
        packed = jnp.where((b_win == g)[:, :, None, None], every_win[:, :, :, g], packed)
    packed = packed.astype(integrals.dtype)
    moved = lax.all_to_all(packed, "redist", split_axis=0, concat_axis=1, tiled=True)[0]

    k_lab = occ_irrep[dev_index * n_rep + rep_index]
    amp = amplitudes[:, 0]
    pair_ik = jnp.bitwise_xor(occ_rows, k_lab)
    per_g = []
    for g in range(N_IRREPS):
        c_irrep = jnp.bitwise_xor(g, k_lab)
        wa = wins[g]
        wc = wins[c_irrep]
        a_lab = lax.dynamic_slice_in_dim(virt_irrep, wa, width)
        cw_lab = lax.dynamic_slice_in_dim(virt_irrep, wc, width)
        a_blk = lax.dynamic_slice(amp, (0, wa, wc), (i_slab, width, width))
        allowed = pair_ik[:, None, None] == jnp.bitwise_xor(a_lab[:, None], cw_lab[None, :])[None]
        a_blk = jnp.where(allowed, a_blk, zero_bf)
        i_blk = lax.dynamic_slice(moved, (wc, 0, 0), (width, j_slab, width))
        sym = (cw_lab == c_irrep)[:, None, None] & (
            jnp.bitwise_xor(cw_lab, k_lab)[:, None, None]
            == jnp.bitwise_xor(occ_js[:, None], a_lab[None, :])[None]
        )
        i_blk = jnp.where(sym, i_blk, zero_bf)
        lhs = jnp.transpose(i_blk, (2, 1, 0)).reshape(width * j_slab, width)
        rhs = a_blk.reshape(i_slab * width, width)
        blk = lax.dot_general(lhs, rhs, (((1,), (1,)), ((), ())), preferred_element_type=jnp.float32)
        per_g.append(blk.reshape(width, -1))
    every = jnp.concatenate(per_g, axis=0)
    b_pos = jnp.arange(v_width, dtype=jnp.int32)
    b_win_start = jnp.zeros_like(virt_irrep)
    for g in range(N_IRREPS):
        b_win_start = jnp.where(virt_irrep == g, wins[g], b_win_start)
    pick = virt_irrep * width + (b_pos - b_win_start)
    compact = jnp.take(every, pick, axis=0, mode="clip")

    n_all = n_redist * n_rep
    nb_all = v_width // n_all
    pieces = lax.all_to_all(compact.reshape(n_all, nb_all, -1), ("redist", "rep"), 0, 0, tiled=True)
    summed = jnp.sum(pieces, axis=0)
    mine_b = lax.all_gather(summed, "rep", axis=0, tiled=True)

    nb = mine_b.shape[0]
    vals = mine_b.reshape(nb, j_slab, i_slab, width).transpose(2, 3, 1, 0)
    my_b_lab = lax.dynamic_slice_in_dim(virt_irrep, dev_index * nb, nb)
    padded = jnp.pad(vals, ((0, 0), (v_width, v_width - width), (0, 0), (0, 0)))
    out = None
    for p in range(parts_in(nb, v_width)):
        lab = my_b_lab[0] + p
        start = v_width - wins[jnp.minimum(lab, N_IRREPS - 1)]
        cut = lax.dynamic_slice_in_dim(padded, start, v_width, axis=1)
        out = cut if out is None else jnp.where((my_b_lab == lab)[None, None, None, :], cut, out)
    return out


def solution(mesh):
    placed = (P(None, ("redist", "rep"), None, None), P(None, "redist", None, None), P(), P())
    return jax.shard_map(
        body, mesh=mesh, in_specs=placed, out_specs=P(None, None, None, "redist"), check_vma=False
    )
```

```python
import jax
import jax.numpy as jnp
from jax import lax
from jax.sharding import PartitionSpec as P

N_IRREPS = 8


def irrep_windows(virt_irrep, width):
    count = virt_irrep.shape[0]
    starts = jnp.sum(
        (virt_irrep[None, :] < jnp.arange(N_IRREPS, dtype=virt_irrep.dtype)[:, None]).astype(jnp.int32),
        axis=1,
    )
    return jnp.minimum(starts, count - width)


def parts_in(span, count):
    return min(N_IRREPS, -(-span // (count // 16)) + 1)


def shifted_pick(array, axis, width, wins, choice):
    out = None
    for g in range(N_IRREPS):
        cut = lax.dynamic_slice_in_dim(array, wins[g], width, axis=axis)
        out = cut if out is None else jnp.where(choice == g, cut, out)
    return out


def body(amplitudes, integrals, occ_irrep, virt_irrep):
    n_redist = lax.axis_size("redist")
    n_rep = lax.axis_size("rep")
    dev_index = lax.axis_index("redist")
    rep_index = lax.axis_index("rep")
    i_slab, k_block, v_width, _ = amplitudes.shape
    c_block = integrals.shape[1]
    j_slab = integrals.shape[2]
    if k_block != 1:
        raise ValueError("unsupported split")
    width = 3 * v_width // 16
    wins = irrep_windows(virt_irrep, width)
    occ_rows = occ_irrep[:i_slab]
    occ_js = occ_irrep[:j_slab]
    zero_bf = jnp.zeros((), amplitudes.dtype)

    grouped = integrals.reshape(n_redist, n_rep, k_block, c_block, j_slab, v_width)
    ints_mine = lax.dynamic_slice_in_dim(grouped, rep_index, 1, 1).reshape(
        n_redist * k_block, c_block, j_slab, v_width
    )
    dest_lab = lax.dynamic_index_in_dim(
        occ_irrep[: n_redist * n_rep].reshape(n_redist, n_rep), rep_index, 1, keepdims=False
    )
    my_c_lab = lax.dynamic_slice_in_dim(virt_irrep, dev_index * c_block, c_block)
    b_win = jnp.bitwise_xor(dest_lab[:, None], my_c_lab[None, :])
    b_iota = jnp.arange(v_width, dtype=jnp.int32)
    t_iota = jnp.arange(width, dtype=jnp.int32)
    selector = (b_iota[None, :, None] == wins[:, None, None] + t_iota[None, None, :]).astype(
        integrals.dtype
    )
    every_win = lax.dot_general(
        ints_mine, selector, (((3,), (1,)), ((), ())), preferred_element_type=jnp.float32
    )
    packed = every_win[:, :, :, 0]
    for g in range(1, N_IRREPS):
        packed = jnp.where((b_win == g)[:, :, None, None], every_win[:, :, :, g], packed)
    packed = packed.astype(integrals.dtype)
    moved = lax.all_to_all(packed, "redist", split_axis=0, concat_axis=1, tiled=True)[0]

    k_lab = occ_irrep[dev_index * n_rep + rep_index]
    amp = amplitudes[:, 0]
    pair_ik = jnp.bitwise_xor(occ_rows, k_lab)
    a_blks = []
    i_blks = []
    for g in range(N_IRREPS):
        c_irrep = jnp.bitwise_xor(g, k_lab)
        wa = wins[g]
        wc = wins[c_irrep]
        a_lab = lax.dynamic_slice_in_dim(virt_irrep, wa, width)
        cw_lab = lax.dynamic_slice_in_dim(virt_irrep, wc, width)
        a_blk = lax.dynamic_slice(amp, (0, wa, wc), (i_slab, width, width))
        allowed = pair_ik[:, None, None] == jnp.bitwise_xor(a_lab[:, None], cw_lab[None, :])[None]
        a_blks.append(jnp.where(allowed, a_blk, zero_bf))
        i_blk = lax.dynamic_slice(moved, (wc, 0, 0), (width, j_slab, width))
        sym = (cw_lab == c_irrep)[:, None, None] & (
            jnp.bitwise_xor(cw_lab, k_lab)[:, None, None]
            == jnp.bitwise_xor(occ_js[:, None], a_lab[None, :])[None]
        )
        i_blks.append(jnp.where(sym, i_blk, zero_bf))
    blk = lax.dot_general(
        jnp.transpose(jnp.stack(i_blks), (0, 3, 2, 1)), jnp.stack(a_blks),
        (((3,), (3,)), ((0,), (0,))), preferred_element_type=jnp.float32,
    )
    every = blk.reshape(N_IRREPS * width, -1)
    b_pos = jnp.arange(v_width, dtype=jnp.int32)
    b_win_start = jnp.zeros_like(virt_irrep)
    for g in range(N_IRREPS):
        b_win_start = jnp.where(virt_irrep == g, wins[g], b_win_start)
    pick = virt_irrep * width + (b_pos - b_win_start)
    compact = jnp.take(every, pick, axis=0, mode="clip")

    n_all = n_redist * n_rep
    nb_all = v_width // n_all
    pieces = lax.all_to_all(compact.reshape(n_all, nb_all, -1), ("redist", "rep"), 0, 0, tiled=True)
    summed = jnp.sum(pieces, axis=0)
    mine_b = lax.all_gather(summed, "rep", axis=0, tiled=True)

    nb = mine_b.shape[0]
    vals = mine_b.reshape(nb, j_slab, i_slab, width).transpose(2, 3, 1, 0)
    my_b_lab = lax.dynamic_slice_in_dim(virt_irrep, dev_index * nb, nb)
    padded = jnp.pad(vals, ((0, 0), (v_width, v_width - width), (0, 0), (0, 0)))
    out = None
    for p in range(parts_in(nb, v_width)):
        lab = my_b_lab[0] + p
        start = v_width - wins[jnp.minimum(lab, N_IRREPS - 1)]
        cut = lax.dynamic_slice_in_dim(padded, start, v_width, axis=1)
        out = cut if out is None else jnp.where((my_b_lab == lab)[None, None, None, :], cut, out)
    return out


def solution(mesh):
    placed = (P(None, ("redist", "rep"), None, None), P(None, "redist", None, None), P(), P())
    return jax.shard_map(
        body, mesh=mesh, in_specs=placed, out_specs=P(None, None, None, "redist"), check_vma=False
    )
```

```python
import jax
import jax.numpy as jnp
from jax import lax
from jax.sharding import PartitionSpec as P

N_IRREPS = 8


def irrep_windows(virt_irrep, width):
    count = virt_irrep.shape[0]
    starts = jnp.sum(
        (virt_irrep[None, :] < jnp.arange(N_IRREPS, dtype=virt_irrep.dtype)[:, None]).astype(jnp.int32),
        axis=1,
    )
    return jnp.minimum(starts, count - width)


def parts_in(span, count):
    return min(N_IRREPS, -(-span // (count // 16)) + 1)


def shifted_pick(array, axis, width, wins, choice):
    out = None
    for g in range(N_IRREPS):
        cut = lax.dynamic_slice_in_dim(array, wins[g], width, axis=axis)
        out = cut if out is None else jnp.where(choice == g, cut, out)
    return out


def body(amplitudes, integrals, occ_irrep, virt_irrep):
    n_redist = lax.axis_size("redist")
    n_rep = lax.axis_size("rep")
    dev_index = lax.axis_index("redist")
    rep_index = lax.axis_index("rep")
    i_slab, k_block, v_width, _ = amplitudes.shape
    c_block = integrals.shape[1]
    j_slab = integrals.shape[2]
    if k_block != 1:
        raise ValueError("unsupported split")
    width = 3 * v_width // 16
    wins = irrep_windows(virt_irrep, width)
    occ_rows = occ_irrep[:i_slab]
    occ_js = occ_irrep[:j_slab]
    zero_bf = jnp.zeros((), amplitudes.dtype)

    grouped = integrals.reshape(n_redist, n_rep, k_block, c_block, j_slab, v_width)
    ints_mine = lax.dynamic_slice_in_dim(grouped, rep_index, 1, 1).reshape(
        n_redist * k_block, c_block, j_slab, v_width
    )
    dest_lab = lax.dynamic_index_in_dim(
        occ_irrep[: n_redist * n_rep].reshape(n_redist, n_rep), rep_index, 1, keepdims=False
    )
    my_c_lab = lax.dynamic_slice_in_dim(virt_irrep, dev_index * c_block, c_block)
    b_win = jnp.bitwise_xor(dest_lab[:, None], my_c_lab[None, :])
    b_iota = jnp.arange(v_width, dtype=jnp.int32)
    t_iota = jnp.arange(width, dtype=jnp.int32)
    selector = (b_iota[None, :, None] == wins[:, None, None] + t_iota[None, None, :]).astype(
        integrals.dtype
    )
    every_win = lax.dot_general(
        ints_mine, selector, (((3,), (1,)), ((), ())), preferred_element_type=jnp.float32
    )
    packed = every_win[:, :, :, 0]
    for g in range(1, N_IRREPS):
        packed = jnp.where((b_win == g)[:, :, None, None], every_win[:, :, :, g], packed)
    packed = packed.astype(integrals.dtype)
    moved = lax.all_to_all(packed, "redist", split_axis=0, concat_axis=1, tiled=True)[0]

    k_lab = occ_irrep[dev_index * n_rep + rep_index]
    amp = amplitudes[:, 0]
    pair_ik = jnp.bitwise_xor(occ_rows, k_lab)
    per_g = []
    for g in range(N_IRREPS):
        c_irrep = jnp.bitwise_xor(g, k_lab)
        wa = wins[g]
        wc = wins[c_irrep]
        a_lab = lax.dynamic_slice_in_dim(virt_irrep, wa, width)
        cw_lab = lax.dynamic_slice_in_dim(virt_irrep, wc, width)
        a_blk = lax.dynamic_slice(amp, (0, wa, wc), (i_slab, width, width))
        allowed = pair_ik[:, None, None] == jnp.bitwise_xor(a_lab[:, None], cw_lab[None, :])[None]
        a_blk = jnp.where(allowed, a_blk, zero_bf)
        i_blk = lax.dynamic_slice(moved, (wc, 0, 0), (width, j_slab, width))
        sym = (cw_lab == c_irrep)[:, None, None] & (
            jnp.bitwise_xor(cw_lab, k_lab)[:, None, None]
            == jnp.bitwise_xor(occ_js[:, None], a_lab[None, :])[None]
        )
        i_blk = jnp.where(sym, i_blk, zero_bf)
        blk = lax.dot_general(
            jnp.transpose(i_blk, (2, 1, 0)), a_blk, (((2,), (2,)), ((), ())),
            preferred_element_type=jnp.float32,
        )
        per_g.append(blk.reshape(width, -1))
    every = jnp.concatenate(per_g, axis=0)
    b_pos = jnp.arange(v_width, dtype=jnp.int32)
    b_win_start = jnp.zeros_like(virt_irrep)
    for g in range(N_IRREPS):
        b_win_start = jnp.where(virt_irrep == g, wins[g], b_win_start)
    pick = virt_irrep * width + (b_pos - b_win_start)
    compact = jnp.take(every, pick, axis=0, mode="clip")

    n_all = n_redist * n_rep
    nb_all = v_width // n_all
    pieces = lax.all_to_all(compact.reshape(n_all, nb_all, -1), ("redist", "rep"), 0, 0, tiled=True)
    summed = jnp.sum(pieces, axis=0)
    got = [summed] + [
        lax.ppermute(summed, "rep", [(z, (z + s) % n_rep) for z in range(n_rep)])
        for s in range(1, n_rep)
    ]
    order = (rep_index - jnp.arange(n_rep, dtype=jnp.int32)) % n_rep
    mine_b = jnp.take(jnp.stack(got), order, axis=0, mode="clip").reshape(n_rep * nb_all, -1)

    nb = mine_b.shape[0]
    vals = mine_b.reshape(nb, j_slab, i_slab, width).transpose(2, 3, 1, 0)
    my_b_lab = lax.dynamic_slice_in_dim(virt_irrep, dev_index * nb, nb)
    padded = jnp.pad(vals, ((0, 0), (v_width, v_width - width), (0, 0), (0, 0)))
    out = None
    for p in range(parts_in(nb, v_width)):
        lab = my_b_lab[0] + p
        start = v_width - wins[jnp.minimum(lab, N_IRREPS - 1)]
        cut = lax.dynamic_slice_in_dim(padded, start, v_width, axis=1)
        out = cut if out is None else jnp.where((my_b_lab == lab)[None, None, None, :], cut, out)
    return out


def solution(mesh):
    placed = (P(None, ("redist", "rep"), None, None), P(None, "redist", None, None), P(), P())
    return jax.shard_map(
        body, mesh=mesh, in_specs=placed, out_specs=P(None, None, None, "redist"), check_vma=False
    )
```

```python
import jax
import jax.numpy as jnp
from jax import lax
from jax.sharding import PartitionSpec as P

N_IRREPS = 8


def irrep_windows(virt_irrep, width):
    count = virt_irrep.shape[0]
    starts = jnp.sum(
        (virt_irrep[None, :] < jnp.arange(N_IRREPS, dtype=virt_irrep.dtype)[:, None]).astype(jnp.int32),
        axis=1,
    )
    return jnp.minimum(starts, count - width)


def parts_in(span, count):
    return min(N_IRREPS, -(-span // (count // 16)) + 1)


def shifted_pick(array, axis, width, wins, choice):
    out = None
    for g in range(N_IRREPS):
        cut = lax.dynamic_slice_in_dim(array, wins[g], width, axis=axis)
        out = cut if out is None else jnp.where(choice == g, cut, out)
    return out


def body(amplitudes, integrals, occ_irrep, virt_irrep):
    n_redist = lax.axis_size("redist")
    n_rep = lax.axis_size("rep")
    dev_index = lax.axis_index("redist")
    rep_index = lax.axis_index("rep")
    i_slab, k_block, v_width, _ = amplitudes.shape
    c_block = integrals.shape[1]
    j_slab = integrals.shape[2]
    if k_block != 1:
        raise ValueError("unsupported split")
    width = 3 * v_width // 16
    wins = irrep_windows(virt_irrep, width)
    occ_rows = occ_irrep[:i_slab]
    occ_js = occ_irrep[:j_slab]
    zero_bf = jnp.zeros((), amplitudes.dtype)

    grouped = integrals.reshape(n_redist, n_rep, k_block, c_block, j_slab, v_width)
    ints_mine = lax.dynamic_slice_in_dim(grouped, rep_index, 1, 1).reshape(
        n_redist * k_block, c_block, j_slab, v_width
    )
    dest_lab = lax.dynamic_index_in_dim(
        occ_irrep[: n_redist * n_rep].reshape(n_redist, n_rep), rep_index, 1, keepdims=False
    )
    my_c_lab = lax.dynamic_slice_in_dim(virt_irrep, dev_index * c_block, c_block)
    b_win = jnp.bitwise_xor(dest_lab[:, None], my_c_lab[None, :])
    b_iota = jnp.arange(v_width, dtype=jnp.int32)
    t_iota = jnp.arange(width, dtype=jnp.int32)
    selector = (b_iota[None, :, None] == wins[:, None, None] + t_iota[None, None, :]).astype(
        integrals.dtype
    )
    every_win = lax.dot_general(
        ints_mine, selector, (((3,), (1,)), ((), ())), preferred_element_type=jnp.float32
    )
    packed = every_win[:, :, :, 0]
    for g in range(1, N_IRREPS):
        packed = jnp.where((b_win == g)[:, :, None, None], every_win[:, :, :, g], packed)
    packed = packed.astype(integrals.dtype)
    got = [
        lax.ppermute(
            lax.dynamic_index_in_dim(packed, (dev_index + s) % n_redist, 0, keepdims=False),
            "redist", [(q, (q + s) % n_redist) for q in range(n_redist)],
        ) if s else lax.dynamic_index_in_dim(packed, dev_index, 0, keepdims=False)
        for s in range(n_redist)
    ]
    src_order = (dev_index - jnp.arange(n_redist, dtype=jnp.int32)) % n_redist
    moved = jnp.take(jnp.stack(got), src_order, axis=0, mode="clip").reshape(
        n_redist * c_block, j_slab, width
    )

    k_lab = occ_irrep[dev_index * n_rep + rep_index]
    amp = amplitudes[:, 0]
    pair_ik = jnp.bitwise_xor(occ_rows, k_lab)
    per_g = []
    for g in range(N_IRREPS):
        c_irrep = jnp.bitwise_xor(g, k_lab)
        wa = wins[g]
        wc = wins[c_irrep]
        a_lab = lax.dynamic_slice_in_dim(virt_irrep, wa, width)
        cw_lab = lax.dynamic_slice_in_dim(virt_irrep, wc, width)
        a_blk = lax.dynamic_slice(amp, (0, wa, wc), (i_slab, width, width))
        allowed = pair_ik[:, None, None] == jnp.bitwise_xor(a_lab[:, None], cw_lab[None, :])[None]
        a_blk = jnp.where(allowed, a_blk, zero_bf)
        i_blk = lax.dynamic_slice(moved, (wc, 0, 0), (width, j_slab, width))
        sym = (cw_lab == c_irrep)[:, None, None] & (
            jnp.bitwise_xor(cw_lab, k_lab)[:, None, None]
            == jnp.bitwise_xor(occ_js[:, None], a_lab[None, :])[None]
        )
        i_blk = jnp.where(sym, i_blk, zero_bf)
        blk = lax.dot_general(
            jnp.transpose(i_blk, (2, 1, 0)), a_blk, (((2,), (2,)), ((), ())),
            preferred_element_type=jnp.float32,
        )
        per_g.append(blk.reshape(width, -1))
    every = jnp.concatenate(per_g, axis=0)
    b_pos = jnp.arange(v_width, dtype=jnp.int32)
    b_win_start = jnp.zeros_like(virt_irrep)
    for g in range(N_IRREPS):
        b_win_start = jnp.where(virt_irrep == g, wins[g], b_win_start)
    pick = virt_irrep * width + (b_pos - b_win_start)
    compact = jnp.take(every, pick, axis=0, mode="clip")

    n_all = n_redist * n_rep
    nb_all = v_width // n_all
    pieces = lax.all_to_all(compact.reshape(n_all, nb_all, -1), ("redist", "rep"), 0, 0, tiled=True)
    summed = jnp.sum(pieces, axis=0)
    got = [summed] + [
        lax.ppermute(summed, "rep", [(z, (z + s) % n_rep) for z in range(n_rep)])
        for s in range(1, n_rep)
    ]
    order = (rep_index - jnp.arange(n_rep, dtype=jnp.int32)) % n_rep
    mine_b = jnp.take(jnp.stack(got), order, axis=0, mode="clip").reshape(n_rep * nb_all, -1)

    nb = mine_b.shape[0]
    vals = mine_b.reshape(nb, j_slab, i_slab, width).transpose(2, 3, 1, 0)
    my_b_lab = lax.dynamic_slice_in_dim(virt_irrep, dev_index * nb, nb)
    padded = jnp.pad(vals, ((0, 0), (v_width, v_width - width), (0, 0), (0, 0)))
    out = None
    for p in range(parts_in(nb, v_width)):
        lab = my_b_lab[0] + p
        start = v_width - wins[jnp.minimum(lab, N_IRREPS - 1)]
        cut = lax.dynamic_slice_in_dim(padded, start, v_width, axis=1)
        out = cut if out is None else jnp.where((my_b_lab == lab)[None, None, None, :], cut, out)
    return out


def solution(mesh):
    placed = (P(None, ("redist", "rep"), None, None), P(None, "redist", None, None), P(), P())
    return jax.shard_map(
        body, mesh=mesh, in_specs=placed, out_specs=P(None, None, None, "redist"), check_vma=False
    )
```
